256 devices in a mesh: dom: 128 (over y, x, z), col: 2 (over core).
Axes of the slice: x: 4, y: 4, z: 8, core: 2. Of those that a mesh axis runs over, the one named last changes fastest.
Arguments:
- src_local: int32 [262144], P('dom'), may hold values from 0 to 4095
- dst_local: int32 [262144], P('dom'), may hold values from 0 to 4095
- edge_weight: float32 [262144], P('dom'), may hold values from 0.25 to 4
- send_counts: int32 [128, 128], P('dom'), may hold values from 1 to 16, as said below
- sketch: bfloat16 [128, 262144], P('col', 'dom'), may hold values from -6 to 6
Outputs:
- solution: float32 [128, 524288], P('col', 'dom')
- resistance: float32 [262144], P('dom')
The draws below stay inside these ranges and needn't reach their ends.
Inputs may be any that keep to these rules, and one draw needn't show every extreme that they name: Each row of send_counts reaches 16 for some peer, and one peer receives 16 live slots from every partition.
All inputs are finite; a program needn't handle non-finite values.
Results may differ from the reference program's by a relative error of at most 0.0003.
Values sent between devices are 32-bit elements; how exact they have to be, the bound alone decides.
No kernel may reach another device: no remote copies, remote signals or barrier semaphores. Data moves between devices by JAX's collectives and lax.ppermute only.
A program may use at most 64 MiB of HBM per device.

```python
import math
import jax
import jax.numpy as jnp
import numpy as np
from jax import lax

SKETCH = 128
VERT_DEV = 4096
EDGE_DEV = 2048
SWEEPS = 3
EDGES = 262144
N_DOM = 128


def draw_send_counts(key, part):
    cap = EDGE_DEV // N_DOM
    levels = cap.bit_length()
    level_key = jax.random.fold_in(key, 11)
    pick_key = jax.random.fold_in(key, 12)
    busy_key = jax.random.fold_in(key, 13)
    coin_key = jax.random.fold_in(key, 14)
    level = jax.random.randint(level_key, (N_DOM, N_DOM), 0, levels)
    coin = jax.random.randint(coin_key, (N_DOM, N_DOM), 0, 2)
    level = level * coin
    counts = jnp.maximum(jnp.right_shift(jnp.full((N_DOM, N_DOM), cap, jnp.int32), level), 1)
    picked = jax.random.randint(pick_key, (N_DOM,), 0, N_DOM)
    busiest = jax.random.randint(busy_key, (), 0, N_DOM)
    columns = jnp.arange(N_DOM)[None, :]
    full = (columns == picked[:, None]) | (columns == busiest)
    return jnp.where(full, cap, counts).astype(jnp.int32)


def set_ends(entries, key, least, high):
    spot = [jax.random.randint(jax.random.fold_in(key, axis), (), 0, length) for axis, length in enumerate(entries.shape)]
    longest = entries.shape.index(max(entries.shape))
    next_to = spot[:longest] + [(spot[longest] + 1) % entries.shape[longest]] + spot[longest + 1:]
    return entries.at[tuple(spot)].set(least).at[tuple(next_to)].set(high)


def block_scale(rng, shape, pieces, low, top_value):
    loudness = 1.0
    for position, shards_of in pieces:
        heights = jax.random.uniform(jax.random.fold_in(jax.random.fold_in(rng, 6), position), (shards_of,), jnp.float32, low / len(pieces), top_value / len(pieces))
        loudness = loudness * jnp.repeat(jnp.exp(heights), shape[position] // shards_of).reshape((-1,) + (1,) * (len(shape) - 1 - position))
    return loudness


def rank_bounds(number_of, slope):
    loads = [(1 << 20) // math.isqrt(standing ** slope) + 1 for standing in range(1, number_of + 1)]
    width = 1 + sum(loads) // (1 << 30)
    return np.cumsum(np.array([max(1, weight // width) for weight in loads]))


def ranked(rng, shape, number_of, lean):
    grid = rank_bounds(number_of, lean)
    pick = jax.random.randint(jax.random.fold_in(rng, 1), shape, 0, int(grid[number_of - 1]))
    rank = jnp.searchsorted(jnp.asarray(grid, jnp.int32), pick, side="right")
    return jax.random.permutation(jax.random.fold_in(rng, 2), number_of)[rank].astype(jnp.int32)


def noise(key, dims, spread, most, split=(), kind=jnp.bfloat16):
    factor_of = block_scale(key, dims, split, -0.22, 0.18) if split else 1.0
    result = jax.random.normal(key, dims, jnp.float32) * spread * factor_of
    return jnp.minimum(jnp.maximum(result, -most), most).astype(kind)


def setup_inputs(seed: int = 0) -> dict:
    arg_keys = jax.random.split(jax.random.key(seed), 6)
    return {
        "src_local": set_ends(ranked(arg_keys[0], (EDGES,), VERT_DEV, 2), jax.random.fold_in(arg_keys[0], 3), 0, VERT_DEV - 1).astype(jnp.int32),
        "dst_local": set_ends(ranked(arg_keys[1], (EDGES,), VERT_DEV, 2), jax.random.fold_in(arg_keys[1], 3), 0, VERT_DEV - 1).astype(jnp.int32),
        "edge_weight": jnp.clip(jnp.exp(math.log(4.0) - 2.7725887 * jax.random.uniform(arg_keys[2], (EDGES,), jnp.float32) ** block_scale(arg_keys[2], (EDGES,), ((0, 128),), -0.2, 0.2)), 0.25, 4.0),
        "send_counts": draw_send_counts(jax.random.fold_in(arg_keys[5], 71), 0),
        "sketch": noise(arg_keys[4], (SKETCH, EDGES), 1.0, 6.0, ((0, 2), (1, 128))),
    }


ground_shift = 1.0
degree_boost = 0.25

def reference(src_local, dst_local, edge_weight, send_counts, sketch):
    cap = EDGE_DEV // N_DOM
    slot = jnp.arange(N_DOM * EDGE_DEV, dtype=jnp.int32)
    owner = slot // EDGE_DEV
    within = slot % EDGE_DEV
    peer = within // cap
    place = within % cap
    live = (place < send_counts[owner, peer]).astype(jnp.float32)
    first = owner * VERT_DEV + src_local
    second = peer * VERT_DEV + dst_local
    weights = edge_weight * live
    count = N_DOM * VERT_DEV
    root = jnp.sqrt(weights)[None, :] * sketch.astype(jnp.float32)
    zero_rows = jnp.zeros((SKETCH, count), jnp.float32)
    rhs = zero_rows.at[:, first].add(root).at[:, second].add(-root)
    degree = jnp.zeros((count,), jnp.float32).at[first].add(weights).at[second].add(weights)
    diag = (1.0 + degree_boost) * degree + ground_shift
    extra = degree_boost * degree + ground_shift

    def apply(field):
        flow = weights[None, :] * (field[:, first] - field[:, second])
        return zero_rows.at[:, first].add(flow).at[:, second].add(-flow) + extra[None, :] * field
    sigma = 1.25
    delta = 0.8
    coeff = 1.0 / sigma
    resid = rhs
    direction = resid / diag[None, :]
    solution = zero_rows
    for sweep in range(SWEEPS):
        solution = solution + direction
        if sweep < SWEEPS - 1:
            resid = resid - apply(direction)
            newer = 1.0 / (2.0 * sigma - coeff)
            direction = newer * coeff * direction + 2.0 * newer / delta * resid / diag[None, :]
            coeff = newer
    diff = solution[:, first] - solution[:, second]
    resistance = lax.optimization_barrier(jnp.sum(diff * diff, axis=0)) / SKETCH * live
    return (solution, resistance)
```

```python
import jax
import jax.numpy as jnp
from jax import lax
from jax.sharding import PartitionSpec as P

SKETCH = 128
VERT_DEV = 4096
SWEEPS = 3


ground_shift = 1.0
degree_boost = 0.25


def local(src_local, dst_local, edge_weight, send_counts, sketch):
    peers = lax.axis_size("dom")
    edges = src_local.shape[0]
    cap = edges // peers
    width = sketch.shape[0]
    live = (jnp.arange(cap)[None, :] < send_counts.reshape(peers, 1)).astype(jnp.float32)
    w_out = (edge_weight.reshape(peers, cap) * live).reshape(-1)
    root = jnp.sqrt(w_out)[:, None] * sketch.astype(jnp.float32).T
    payload = jnp.concatenate(
        [root, w_out[:, None], dst_local.astype(jnp.float32)[:, None]], axis=1
    )
    arrived = lax.all_to_all(payload, "dom", split_axis=0, concat_axis=0, tiled=True)
    arrived_root = arrived[:, :width]
    w_in = arrived[:, width]
    wanted = arrived[:, width + 1].astype(jnp.int32)

    both = jnp.stack(
        [src_local.reshape(peers, cap), wanted.reshape(peers, cap)], axis=1
    ).reshape(-1)
    zero_rows = jnp.zeros((VERT_DEV, width), jnp.float32)
    rhs = zero_rows.at[both].add(
        jnp.stack(
            [root.reshape(peers, cap, width), -arrived_root.reshape(peers, cap, width)],
            axis=1,
        ).reshape(-1, width)
    )
    w_both = jnp.stack([w_out.reshape(peers, cap), w_in.reshape(peers, cap)], axis=1).reshape(-1)
    degree = jnp.zeros((VERT_DEV,), jnp.float32).at[both].add(w_both)
    diag = ((1.0 + degree_boost) * degree + ground_shift)[:, None]
    extra = (degree_boost * degree + ground_shift)[:, None]

    def apply(field):
        here = field[both].reshape(peers, 2, cap, width)
        there = lax.all_to_all(here, "dom", split_axis=0, concat_axis=0, tiled=True)
        flow_out = w_out.reshape(peers, cap, 1) * (here[:, 0] - there[:, 1])
        flow_in = w_in.reshape(peers, cap, 1) * (there[:, 0] - here[:, 1])
        flows = jnp.stack([flow_out, -flow_in], axis=1).reshape(-1, width)
        return zero_rows.at[both].add(flows) + extra * field

    sigma = 1.25
    delta = 0.8
    coeff = 1.0 / sigma
    resid = rhs
    direction = resid / diag
    solution = zero_rows
    for sweep in range(SWEEPS):
        solution = solution + direction
        if sweep < SWEEPS - 1:
            resid = resid - apply(direction)
            newer = 1.0 / (2.0 * sigma - coeff)
            direction = newer * coeff * direction + 2.0 * newer / delta * resid / diag
            coeff = newer
    far = lax.all_to_all(
        solution[wanted], "dom", split_axis=0, concat_axis=0, tiled=True
    )
    diff = solution[src_local] - far
    partial_sum = jnp.sum(diff * diff, axis=1) * live.reshape(-1)
    resistance = lax.psum(partial_sum, "col") / SKETCH
    return (solution.T, resistance)


def solution(mesh):
    in_specs = (P("dom"), P("dom"), P("dom"), P("dom", None), P("col", "dom"))
    out_specs = (P("col", "dom"), P("dom"))
    return jax.shard_map(local, mesh=mesh, in_specs=in_specs, out_specs=out_specs, check_vma=False)
```

```python
import functools

import jax
import jax.numpy as jnp
from jax import lax
from jax.experimental import pallas as pl
from jax.experimental.pallas import tpu as pltpu
from jax.sharding import PartitionSpec as P

SKETCH = 128
VERT_DEV = 4096
SWEEPS = 3
BLOCK = 16


ground_shift = 1.0
degree_boost = 0.25


def _pair_gather_kernel(a_ref, b_ref, x_ref, o_ref):
    lanes = x_ref.shape[2]
    low = lax.broadcasted_iota(jnp.int32, (1, lanes), 1) < lanes // 2

    def body(t, carry):
        base = t * BLOCK
        rows = [(x_ref[a_ref[base + r]], x_ref[b_ref[base + r]]) for r in range(BLOCK)]
        for r in range(BLOCK):
            o_ref[base + r] = jnp.where(low, rows[r][0], rows[r][1])
        return carry

    lax.fori_loop(0, o_ref.shape[0] // BLOCK, body, 0)


def pair_gather(a, b, x):
    return pl.pallas_call(
        _pair_gather_kernel,
        out_shape=jax.ShapeDtypeStruct((a.shape[0],) + x.shape[1:], x.dtype),
        in_specs=[
            pl.BlockSpec(memory_space=pltpu.SMEM),
            pl.BlockSpec(memory_space=pltpu.SMEM),
            pl.BlockSpec(memory_space=pltpu.VMEM),
        ],
        out_specs=pl.BlockSpec(memory_space=pltpu.VMEM),
    )(a, b, x)


def _sorted_scatter_kernel(half, key_ref, slot_ref, side_ref, v_ref, o_ref):
    lanes = o_ref.shape[2]
    o_ref[...] = jnp.zeros(o_ref.shape, o_ref.dtype)
    group = (lax.broadcasted_iota(jnp.int32, (1, lanes), 1) // half) % 2

    def body(t, carry):
        run, prev = carry
        base = t * BLOCK
        rows = [v_ref[slot_ref[base + r]] for r in range(BLOCK)]
        for r in range(BLOCK):
            i = base + r
            k = key_ref[i]
            mine = jnp.where(group == side_ref[i], rows[r], jnp.zeros_like(rows[r]))
            run = jnp.where(k == prev, run, jnp.zeros_like(run)) + mine
            o_ref[k] = run
            prev = k
        return run, prev

    lax.fori_loop(
        0,
        key_ref.shape[0] // BLOCK,
        body,
        (jnp.zeros((1, lanes), jnp.float32), jnp.int32(-1)),
    )


def sorted_scatter(half, key, slot, side, vals, rows):
    return pl.pallas_call(
        functools.partial(_sorted_scatter_kernel, half),
        out_shape=jax.ShapeDtypeStruct((rows,) + vals.shape[1:], vals.dtype),
        in_specs=[
            pl.BlockSpec(memory_space=pltpu.SMEM),
            pl.BlockSpec(memory_space=pltpu.SMEM),
            pl.BlockSpec(memory_space=pltpu.SMEM),
            pl.BlockSpec(memory_space=pltpu.VMEM),
        ],
        out_specs=pl.BlockSpec(memory_space=pltpu.VMEM),
    )(key, slot, side, vals)


def local(src_local, dst_local, edge_weight, send_counts, sketch):
    peers = lax.axis_size("dom")
    edges = src_local.shape[0]
    cap = edges // peers
    width = sketch.shape[0]

    def a2a(x):
        return lax.all_to_all(x, "dom", split_axis=0, concat_axis=0, tiled=True)

    live = (jnp.arange(cap)[None, :] < send_counts.reshape(peers, 1)).astype(jnp.float32)
    w_out = (edge_weight.reshape(peers, cap) * live).reshape(-1)
    root = jnp.sqrt(w_out)[:, None] * sketch.astype(jnp.float32).T
    payload = jnp.concatenate(
        [root, w_out[:, None], dst_local.astype(jnp.float32)[:, None]], axis=1
    )
    arrived = a2a(payload)
    arrived_root = arrived[:, :width]
    w_in = arrived[:, width]
    wanted = arrived[:, width + 1].astype(jnp.int32)

    keys = jnp.stack([src_local, wanted], axis=1).reshape(-1)
    key_s, entry_s = lax.sort(
        (keys, jnp.arange(2 * edges, dtype=jnp.int32)), num_keys=1
    )
    slot_s = entry_s // 2
    side_s = entry_s % 2

    def scatter(vals):
        return sorted_scatter(width, key_s, slot_s, side_s, vals, VERT_DEV)

    ones = jnp.ones((1, width), jnp.float32)
    first = jnp.concatenate(
        [root, -arrived_root, w_out[:, None] * ones, w_in[:, None] * ones], axis=1
    ).reshape(edges, 1, 4 * width)
    acc = scatter(first).reshape(VERT_DEV, 4 * width)
    rhs = acc[:, :width] + acc[:, width:2 * width]
    degree = acc[:, 2 * width] + acc[:, 3 * width]
    diag = ((1.0 + degree_boost) * degree + ground_shift)[:, None]
    extra = (degree_boost * degree + ground_shift)[:, None]

    def ends(field):
        doubled = jnp.concatenate([field, field], axis=1).reshape(VERT_DEV, 1, 2 * width)
        return pair_gather(src_local, wanted, doubled)

    def apply(field):
        here = ends(field)
        there = a2a(here).reshape(edges, 2 * width)
        here = here.reshape(edges, 2 * width)
        flow_out = w_out[:, None] * (here[:, :width] - there[:, width:])
        flow_in = w_in[:, None] * (there[:, :width] - here[:, width:])
        flows = jnp.concatenate([flow_out, -flow_in], axis=1).reshape(edges, 1, 2 * width)
        acc = scatter(flows).reshape(VERT_DEV, 2 * width)
        return (acc[:, :width] + acc[:, width:]) + extra * field

    sigma = 1.25
    delta = 0.8
    coeff = 1.0 / sigma
    resid = rhs
    direction = resid / diag
    solution = jnp.zeros((VERT_DEV, width), jnp.float32)
    for sweep in range(SWEEPS):
        solution = solution + direction
        if sweep < SWEEPS - 1:
            resid = resid - apply(direction)
            newer = 1.0 / (2.0 * sigma - coeff)
            direction = newer * coeff * direction + 2.0 * newer / delta * resid / diag
            coeff = newer
    here = ends(solution).reshape(edges, 2 * width)
    far = a2a(here[:, width:].reshape(edges // 2, 2 * width)).reshape(edges, width)
    diff = here[:, :width] - far
    partial_sum = jnp.sum(diff * diff, axis=1) * live.reshape(-1)
    resistance = lax.psum(partial_sum, "col") / SKETCH
    return (solution.T, resistance)


def solution(mesh):
    in_specs = (P("dom"), P("dom"), P("dom"), P("dom", None), P("col", "dom"))
    out_specs = (P("col", "dom"), P("dom"))
    return jax.shard_map(local, mesh=mesh, in_specs=in_specs, out_specs=out_specs, check_vma=False)
```

```python
import functools

import jax
import jax.numpy as jnp
from jax import lax
from jax.experimental import pallas as pl
from jax.experimental.pallas import tpu as pltpu
from jax.sharding import PartitionSpec as P

SKETCH = 128
VERT_DEV = 4096
SWEEPS = 3
BLOCK = 16
RUN_BLOCK = 4


ground_shift = 1.0
degree_boost = 0.25


def _pair_gather_kernel(a_ref, b_ref, x_ref, o_ref):
    lanes = x_ref.shape[2]
    low = lax.broadcasted_iota(jnp.int32, (1, lanes), 1) < lanes // 2

    def body(t, carry):
        base = t * BLOCK
        rows = [(x_ref[a_ref[base + r]], x_ref[b_ref[base + r]]) for r in range(BLOCK)]
        for r in range(BLOCK):
            o_ref[base + r] = jnp.where(low, rows[r][0], rows[r][1])
        return carry

    lax.fori_loop(0, o_ref.shape[0] // BLOCK, body, 0)


def pair_gather(a, b, x):
    return pl.pallas_call(
        _pair_gather_kernel,
        out_shape=jax.ShapeDtypeStruct((a.shape[0],) + x.shape[1:], x.dtype),
        in_specs=[
            pl.BlockSpec(memory_space=pltpu.SMEM),
            pl.BlockSpec(memory_space=pltpu.SMEM),
            pl.BlockSpec(memory_space=pltpu.VMEM),
        ],
        out_specs=pl.BlockSpec(memory_space=pltpu.VMEM),
    )(a, b, x)


def _sorted_scatter_kernel(key_ref, slot_ref, v0_ref, v1_ref, s0_ref, s1_ref, t0_ref, t1_ref):
    lanes = s0_ref.shape[2]
    rows = s0_ref.shape[0]
    n = key_ref.shape[0] // 4
    outs = (s0_ref, t0_ref, s1_ref, t1_ref)
    vals = (v0_ref, v0_ref, v1_ref, v1_ref)
    step = 64

    @pl.loop(0, rows // step)
    def _(i):
        at = pl.ds(pl.multiple_of(i * step, step), step)
        for o in outs:
            o[at] = jnp.zeros((step,) + o.shape[1:], o.dtype)

    def body(t, carry):
        runs, prevs = carry
        runs, prevs = list(runs), list(prevs)
        base = t * RUN_BLOCK
        got = [
            [vals[c][slot_ref[c * n + base + r]] for c in range(4)] for r in range(RUN_BLOCK)
        ]
        for r in range(RUN_BLOCK):
            for c in range(4):
                k = key_ref[c * n + base + r]
                runs[c] = jnp.where(k == prevs[c], runs[c], jnp.zeros_like(runs[c])) + got[r][c]
                outs[c][k] = runs[c]
                prevs[c] = k
        return tuple(runs), tuple(prevs)

    zero = jnp.zeros((1, lanes), jnp.float32)
    lax.fori_loop(0, n // RUN_BLOCK, body, ((zero,) * 4, (jnp.int32(-1),) * 4))

    @pl.loop(0, rows // step)
    def _(i):
        at = pl.ds(pl.multiple_of(i * step, step), step)
        s0_ref[at] += t0_ref[at]
        s1_ref[at] += t1_ref[at]


def sorted_scatter(key, slot, v0, v1, rows):
    shape = jax.ShapeDtypeStruct((rows,) + v0.shape[1:], v0.dtype)
    return pl.pallas_call(
        _sorted_scatter_kernel,
        out_shape=(shape, shape),
        in_specs=[
            pl.BlockSpec(memory_space=pltpu.SMEM),
            pl.BlockSpec(memory_space=pltpu.SMEM),
            pl.BlockSpec(memory_space=pltpu.VMEM),
            pl.BlockSpec(memory_space=pltpu.VMEM),
        ],
        out_specs=(pl.BlockSpec(memory_space=pltpu.VMEM), pl.BlockSpec(memory_space=pltpu.VMEM)),
        scratch_shapes=[pltpu.VMEM((rows,) + v0.shape[1:], v0.dtype)] * 2,
    )(key, slot, v0, v1)


def local(src_local, dst_local, edge_weight, send_counts, sketch):
    peers = lax.axis_size("dom")
    edges = src_local.shape[0]
    cap = edges // peers
    width = sketch.shape[0]

    def a2a(x):
        return lax.all_to_all(x, "dom", split_axis=0, concat_axis=0, tiled=True)

    live = (jnp.arange(cap)[None, :] < send_counts.reshape(peers, 1)).astype(jnp.float32)
    w_out = (edge_weight.reshape(peers, cap) * live).reshape(-1)
    root = jnp.sqrt(w_out)[:, None] * sketch.astype(jnp.float32).T
    lanes = 2 * width
    side_row = jnp.concatenate(
        [
            w_out.reshape(peers, 1, cap),
            dst_local.astype(jnp.float32).reshape(peers, 1, cap),
            jnp.zeros((peers, 1, lanes - 2 * cap), jnp.float32),
        ],
        axis=2,
    )
    payload = jnp.concatenate([root.reshape(peers, -1, lanes), side_row], axis=1)
    arrived = a2a(payload)
    arrived_root = arrived[:, :-1].reshape(edges, width)
    w_in = arrived[:, -1, :cap].reshape(-1)
    wanted = arrived[:, -1, cap:2 * cap].reshape(-1).astype(jnp.int32)

    keys = jnp.concatenate([src_local, wanted + VERT_DEV])
    key_s, entry_s = lax.sort(
        (keys, jnp.arange(2 * edges, dtype=jnp.int32)), num_keys=1
    )
    key_s = key_s % VERT_DEV
    slot_s = entry_s % edges

    def scatter(v0, v1):
        s0, s1 = sorted_scatter(key_s, slot_s, v0, v1, VERT_DEV)
        return s0.reshape(VERT_DEV, lanes), s1.reshape(VERT_DEV, lanes)

    ones = jnp.ones((1, width), jnp.float32)
    s0, s1 = scatter(
        jnp.concatenate([root, w_out[:, None] * ones], axis=1).reshape(edges, 1, lanes),
        jnp.concatenate([-arrived_root, w_in[:, None] * ones], axis=1).reshape(edges, 1, lanes),
    )
    rhs = s0[:, :width] + s1[:, :width]
    degree = s0[:, width] + s1[:, width]
    diag = ((1.0 + degree_boost) * degree + ground_shift)[:, None]
    extra = (degree_boost * degree + ground_shift)[:, None]

    def ends(field):
        doubled = jnp.concatenate([field, field], axis=1).reshape(VERT_DEV, 1, 2 * width)
        return pair_gather(src_local, wanted, doubled)

    def apply(field):
        here = ends(field)
        there = a2a(here).reshape(edges, 2 * width)
        here = here.reshape(edges, 2 * width)
        flow_out = w_out[:, None] * (here[:, :width] - there[:, width:])
        flow_in = w_in[:, None] * (there[:, :width] - here[:, width:])
        flows = jnp.concatenate([flow_out, -flow_in], axis=1).reshape(edges, 1, lanes)
        s0, s1 = scatter(flows, flows)
        return (s0[:, :width] + s1[:, width:]) + extra * field

    sigma = 1.25
    delta = 0.8
    coeff = 1.0 / sigma
    resid = rhs
    direction = resid / diag
    solution = jnp.zeros((VERT_DEV, width), jnp.float32)
    for sweep in range(SWEEPS):
        solution = solution + direction
        if sweep < SWEEPS - 1:
            resid = resid - apply(direction)
            newer = 1.0 / (2.0 * sigma - coeff)
            direction = newer * coeff * direction + 2.0 * newer / delta * resid / diag
            coeff = newer
    here = ends(solution).reshape(edges, 2 * width)
    far = a2a(here[:, width:].reshape(edges // 2, 2 * width)).reshape(edges, width)
    diff = here[:, :width] - far
    partial_sum = jnp.sum(diff * diff, axis=1) * live.reshape(-1)
    resistance = lax.psum(partial_sum, "col") / SKETCH
    return (solution.T, resistance)


def solution(mesh):
    in_specs = (P("dom"), P("dom"), P("dom"), P("dom", None), P("col", "dom"))
    out_specs = (P("col", "dom"), P("dom"))
    return jax.shard_map(local, mesh=mesh, in_specs=in_specs, out_specs=out_specs, check_vma=False)
```

```python
import functools

import jax
import jax.numpy as jnp
from jax import lax
from jax.experimental import pallas as pl
from jax.experimental.pallas import tpu as pltpu
from jax.sharding import PartitionSpec as P

SKETCH = 128
VERT_DEV = 4096
SWEEPS = 3
BLOCK = 16
RUN_BLOCK = 8


ground_shift = 1.0
degree_boost = 0.25


def _pair_gather_kernel(half, a_ref, b_ref, x_ref, o_ref):
    lanes = x_ref.shape[2]
    low = (lax.broadcasted_iota(jnp.int32, (1, lanes), 1) // half) % 2 == 0

    def body(t, carry):
        base = t * BLOCK
        rows = [(x_ref[a_ref[base + r]], x_ref[b_ref[base + r]]) for r in range(BLOCK)]
        for r in range(BLOCK):
            o_ref[base + r] = jnp.where(low, rows[r][0], rows[r][1])
        return carry

    lax.fori_loop(0, o_ref.shape[0] // BLOCK, body, 0)


def pair_gather(a, b, x, half):
    return pl.pallas_call(
        functools.partial(_pair_gather_kernel, half),
        out_shape=jax.ShapeDtypeStruct((a.shape[0],) + x.shape[1:], x.dtype),
        in_specs=[
            pl.BlockSpec(memory_space=pltpu.SMEM),
            pl.BlockSpec(memory_space=pltpu.SMEM),
            pl.BlockSpec(memory_space=pltpu.VMEM),
        ],
        out_specs=pl.BlockSpec(memory_space=pltpu.VMEM),
    )(a, b, x)


def _runs_kernel(k0_ref, k1_ref, v_ref, o0_ref, o1_ref):
    lanes = v_ref.shape[2]
    rows = o0_ref.shape[0]
    step = 64

    @pl.loop(0, rows // step)
    def _(i):
        at = pl.ds(pl.multiple_of(i * step, step), step)
        o0_ref[at] = jnp.zeros((step,) + o0_ref.shape[1:], o0_ref.dtype)
        o1_ref[at] = jnp.zeros((step,) + o1_ref.shape[1:], o1_ref.dtype)

    def body(t, carry):
        r0, r1, p0, p1 = carry
        base = t * RUN_BLOCK
        got = [v_ref[base + r] for r in range(RUN_BLOCK)]
        for r in range(RUN_BLOCK):
            k0 = k0_ref[base + r]
            k1 = k1_ref[base + r]
            r0 = jnp.where(k0 == p0, r0, jnp.zeros_like(r0)) + got[r]
            r1 = jnp.where(k1 == p1, r1, jnp.zeros_like(r1)) + got[r]
            o0_ref[k0] = r0
            o1_ref[k1] = r1
            p0, p1 = k0, k1
        return r0, r1, p0, p1

    zero = jnp.zeros((1, lanes), jnp.float32)
    lax.fori_loop(
        0, v_ref.shape[0] // RUN_BLOCK, body, (zero, zero, jnp.int32(-1), jnp.int32(-1))
    )


def runs(k0, k1, v, rows):
    shape = jax.ShapeDtypeStruct((rows,) + v.shape[1:], v.dtype)
    return pl.pallas_call(
        _runs_kernel,
        out_shape=(shape, shape),
        in_specs=[
            pl.BlockSpec(memory_space=pltpu.SMEM),
            pl.BlockSpec(memory_space=pltpu.SMEM),
            pl.BlockSpec(memory_space=pltpu.VMEM),
        ],
        out_specs=(pl.BlockSpec(memory_space=pltpu.VMEM), pl.BlockSpec(memory_space=pltpu.VMEM)),
    )(k0, k1, v)


def local(src_local, dst_local, edge_weight, send_counts, sketch):
    peers = lax.axis_size("dom")
    edges = src_local.shape[0]
    cap = edges // peers
    width = sketch.shape[0]

    def a2a(x):
        return lax.all_to_all(x, "dom", split_axis=0, concat_axis=0, tiled=True)

    live = (jnp.arange(cap)[None, :] < send_counts.reshape(peers, 1)).astype(jnp.float32)
    w_out = (edge_weight.reshape(peers, cap) * live).reshape(-1)
    root = jnp.sqrt(w_out)[:, None] * sketch.astype(jnp.float32).T
    lanes = 2 * width
    side_row = jnp.concatenate(
        [
            w_out.reshape(peers, 1, cap),
            dst_local.astype(jnp.float32).reshape(peers, 1, cap),
            jnp.zeros((peers, 1, lanes - 2 * cap), jnp.float32),
        ],
        axis=2,
    )
    payload = jnp.concatenate([root.reshape(peers, -1, lanes), side_row], axis=1)
    arrived = a2a(payload)
    arrived_root = arrived[:, :-1].reshape(edges, width)
    w_in = arrived[:, -1, :cap].reshape(-1)
    wanted = arrived[:, -1, cap:2 * cap].reshape(-1).astype(jnp.int32)

    keys = jnp.concatenate([src_local, wanted + VERT_DEV])
    key_s, entry_s = lax.sort(
        (keys, jnp.arange(2 * edges, dtype=jnp.int32)), num_keys=1
    )
    key_0, key_1 = key_s[:edges], key_s[edges:] - VERT_DEV
    slot_0, slot_1 = entry_s[:edges], entry_s[edges:] - edges

    def scatter(vals, half):
        ordered = pair_gather(slot_0, slot_1, vals, half)
        s0, s1 = runs(key_0, key_1, ordered, VERT_DEV)
        return s0.reshape(VERT_DEV, -1), s1.reshape(VERT_DEV, -1)

    ones = jnp.ones((1, width), jnp.float32)
    s0, s1 = scatter(
        jnp.concatenate(
            [root, -arrived_root, w_out[:, None] * ones, w_in[:, None] * ones], axis=1
        ).reshape(edges, 1, 2 * lanes),
        width,
    )
    rhs = s0[:, :width] + s1[:, width:lanes]
    degree = s0[:, lanes] + s1[:, lanes + width]
    diag = ((1.0 + degree_boost) * degree + ground_shift)[:, None]
    extra = (degree_boost * degree + ground_shift)[:, None]

    def ends(field):
        doubled = jnp.concatenate([field, field], axis=1).reshape(VERT_DEV, 1, 2 * width)
        return pair_gather(src_local, wanted, doubled, width)

    def apply(field):
        here = ends(field)
        there = a2a(here).reshape(edges, 2 * width)
        here = here.reshape(edges, 2 * width)
        flow_out = w_out[:, None] * (here[:, :width] - there[:, width:])
        flow_in = w_in[:, None] * (there[:, :width] - here[:, width:])
        flows = jnp.concatenate([flow_out, -flow_in], axis=1).reshape(edges, 1, lanes)
        s0, s1 = scatter(flows, width)
        return (s0[:, :width] + s1[:, width:]) + extra * field

    sigma = 1.25
    delta = 0.8
    coeff = 1.0 / sigma
    resid = rhs
    direction = resid / diag
    solution = jnp.zeros((VERT_DEV, width), jnp.float32)
    for sweep in range(SWEEPS):
        solution = solution + direction
        if sweep < SWEEPS - 1:
            resid = resid - apply(direction)
            newer = 1.0 / (2.0 * sigma - coeff)
            direction = newer * coeff * direction + 2.0 * newer / delta * resid / diag
            coeff = newer
    here = ends(solution).reshape(edges, 2 * width)
    far = a2a(here[:, width:].reshape(edges // 2, 2 * width)).reshape(edges, width)
    diff = here[:, :width] - far
    partial_sum = jnp.sum(diff * diff, axis=1) * live.reshape(-1)
    resistance = lax.psum(partial_sum, "col") / SKETCH
    return (solution.T, resistance)


def solution(mesh):
    in_specs = (P("dom"), P("dom"), P("dom"), P("dom", None), P("col", "dom"))
    out_specs = (P("col", "dom"), P("dom"))
    return jax.shard_map(local, mesh=mesh, in_specs=in_specs, out_specs=out_specs, check_vma=False)
```

```python
import functools

import jax
import jax.numpy as jnp
from jax import lax
from jax.experimental import pallas as pl
from jax.experimental.pallas import tpu as pltpu
from jax.sharding import PartitionSpec as P

SKETCH = 128
VERT_DEV = 4096
SWEEPS = 3
BLOCK = 16


ground_shift = 1.0
degree_boost = 0.25


def _pair_gather_kernel(a_ref, b_ref, x_ref, o_ref):
    lanes = x_ref.shape[2]
    low = lax.broadcasted_iota(jnp.int32, (1, lanes), 1) < lanes // 2

    def body(t, carry):
        base = t * BLOCK
        rows = [(x_ref[a_ref[base + r]], x_ref[b_ref[base + r]]) for r in range(BLOCK)]
        for r in range(BLOCK):
            o_ref[base + r] = jnp.where(low, rows[r][0], rows[r][1])
        return carry

    lax.fori_loop(0, o_ref.shape[0] // BLOCK, body, 0)


def pair_gather(a, b, x):
    return pl.pallas_call(
        _pair_gather_kernel,
        out_shape=jax.ShapeDtypeStruct((a.shape[0],) + x.shape[1:], x.dtype),
        in_specs=[
            pl.BlockSpec(memory_space=pltpu.SMEM),
            pl.BlockSpec(memory_space=pltpu.SMEM),
            pl.BlockSpec(memory_space=pltpu.VMEM),
        ],
        out_specs=pl.BlockSpec(memory_space=pltpu.VMEM),
    )(a, b, x)


def _sorted_scatter_kernel(half, key_ref, slot_ref, side_ref, v_ref, o_ref):
    lanes = o_ref.shape[2]
    step = 64

    @pl.loop(0, o_ref.shape[0] // step)
    def _(i):
        at = pl.ds(pl.multiple_of(i * step, step), step)
        o_ref[at] = jnp.zeros((step,) + o_ref.shape[1:], o_ref.dtype)
    group = (lax.broadcasted_iota(jnp.int32, (1, lanes), 1) // half) % 2

    def body(t, carry):
        run, prev = carry
        base = t * BLOCK
        rows = [v_ref[slot_ref[base + r]] for r in range(BLOCK)]
        for r in range(BLOCK):
            i = base + r
            k = key_ref[i]
            mine = jnp.where(group == side_ref[i], rows[r], jnp.zeros_like(rows[r]))
            run = jnp.where(k == prev, run, jnp.zeros_like(run)) + mine
            o_ref[k] = run
            prev = k
        return run, prev

    lax.fori_loop(
        0,
        key_ref.shape[0] // BLOCK,
        body,
        (jnp.zeros((1, lanes), jnp.float32), jnp.int32(-1)),
    )


def sorted_scatter(half, key, slot, side, vals, rows):
    return pl.pallas_call(
        functools.partial(_sorted_scatter_kernel, half),
        out_shape=jax.ShapeDtypeStruct((rows,) + vals.shape[1:], vals.dtype),
        in_specs=[
            pl.BlockSpec(memory_space=pltpu.SMEM),
            pl.BlockSpec(memory_space=pltpu.SMEM),
            pl.BlockSpec(memory_space=pltpu.SMEM),
            pl.BlockSpec(memory_space=pltpu.VMEM),
        ],
        out_specs=pl.BlockSpec(memory_space=pltpu.VMEM),
    )(key, slot, side, vals)


def local(src_local, dst_local, edge_weight, send_counts, sketch):
    peers = lax.axis_size("dom")
    edges = src_local.shape[0]
    cap = edges // peers
    width = sketch.shape[0]

    def a2a(x):
        return lax.all_to_all(x, "dom", split_axis=0, concat_axis=0, tiled=True)

    live = (jnp.arange(cap)[None, :] < send_counts.reshape(peers, 1)).astype(jnp.float32)
    w_out = (edge_weight.reshape(peers, cap) * live).reshape(-1)
    root = jnp.sqrt(w_out)[:, None] * sketch.astype(jnp.float32).T
    lanes = 2 * width
    side_row = jnp.concatenate(
        [
            w_out.reshape(peers, 1, cap),
            dst_local.astype(jnp.float32).reshape(peers, 1, cap),
            jnp.zeros((peers, 1, lanes - 2 * cap), jnp.float32),
        ],
        axis=2,
    )
    payload = jnp.concatenate([root.reshape(peers, -1, lanes), side_row], axis=1)
    arrived = a2a(payload)
    arrived_root = arrived[:, :-1].reshape(edges, width)
    w_in = arrived[:, -1, :cap].reshape(-1)
    wanted = arrived[:, -1, cap:2 * cap].reshape(-1).astype(jnp.int32)

    keys = jnp.stack([src_local, wanted], axis=1).reshape(-1)
    key_s, entry_s = lax.sort(
        (keys, jnp.arange(2 * edges, dtype=jnp.int32)), num_keys=1
    )
    slot_s = entry_s // 2
    side_s = entry_s % 2

    def scatter(vals):
        return sorted_scatter(width, key_s, slot_s, side_s, vals, VERT_DEV).reshape(
            VERT_DEV, -1
        )

    ones = jnp.ones((1, width), jnp.float32)
    acc = scatter(
        jnp.concatenate(
            [root, -arrived_root, w_out[:, None] * ones, w_in[:, None] * ones], axis=1
        ).reshape(edges, 1, 2 * lanes)
    )
    rhs = acc[:, :width] + acc[:, width:lanes]
    degree = acc[:, lanes] + acc[:, lanes + width]
    diag = ((1.0 + degree_boost) * degree + ground_shift)[:, None]
    extra = (degree_boost * degree + ground_shift)[:, None]

    def ends(field):
        doubled = jnp.concatenate([field, field], axis=1).reshape(VERT_DEV, 1, 2 * width)
        return pair_gather(src_local, wanted, doubled)

    def apply(field):
        here = ends(field)
        there = a2a(here).reshape(edges, 2 * width)
        here = here.reshape(edges, 2 * width)
        flow_out = w_out[:, None] * (here[:, :width] - there[:, width:])
        flow_in = w_in[:, None] * (there[:, :width] - here[:, width:])
        flows = jnp.concatenate([flow_out, -flow_in], axis=1).reshape(edges, 1, lanes)
        acc = scatter(flows)
        return (acc[:, :width] + acc[:, width:]) + extra * field

    sigma = 1.25
    delta = 0.8
    coeff = 1.0 / sigma
    resid = rhs
    direction = resid / diag
    solution = jnp.zeros((VERT_DEV, width), jnp.float32)
    for sweep in range(SWEEPS):
        solution = solution + direction
        if sweep < SWEEPS - 1:
            resid = resid - apply(direction)
            newer = 1.0 / (2.0 * sigma - coeff)
            direction = newer * coeff * direction + 2.0 * newer / delta * resid / diag
            coeff = newer
    here = ends(solution).reshape(edges, 2 * width)
    far = a2a(here[:, width:].reshape(edges // 2, 2 * width)).reshape(edges, width)
    diff = here[:, :width] - far
    partial_sum = jnp.sum(diff * diff, axis=1) * live.reshape(-1)
    resistance = lax.psum(partial_sum, "col") / SKETCH
    return (solution.T, resistance)


def solution(mesh):
    in_specs = (P("dom"), P("dom"), P("dom"), P("dom", None), P("col", "dom"))
    out_specs = (P("col", "dom"), P("dom"))
    return jax.shard_map(local, mesh=mesh, in_specs=in_specs, out_specs=out_specs, check_vma=False)
```

```python
import functools

import jax
import jax.numpy as jnp
from jax import lax
from jax.experimental import pallas as pl
from jax.experimental.pallas import tpu as pltpu
from jax.sharding import PartitionSpec as P

SKETCH = 128
VERT_DEV = 4096
SWEEPS = 3
BLOCK = 16
CHUNKS = 2


ground_shift = 1.0
degree_boost = 0.25


def _pair_gather_kernel(a_ref, b_ref, x_ref, o_ref):
    lanes = x_ref.shape[2]
    low = lax.broadcasted_iota(jnp.int32, (1, lanes), 1) < lanes // 2

    def body(t, carry):
        base = t * BLOCK
        rows = [(x_ref[a_ref[base + r]], x_ref[b_ref[base + r]]) for r in range(BLOCK)]
        for r in range(BLOCK):
            o_ref[base + r] = jnp.where(low, rows[r][0], rows[r][1])
        return carry

    lax.fori_loop(0, o_ref.shape[0] // BLOCK, body, 0)


def pair_gather(a, b, x):
    return pl.pallas_call(
        _pair_gather_kernel,
        out_shape=jax.ShapeDtypeStruct((a.shape[0],) + x.shape[1:], x.dtype),
        in_specs=[
            pl.BlockSpec(memory_space=pltpu.SMEM),
            pl.BlockSpec(memory_space=pltpu.SMEM),
            pl.BlockSpec(memory_space=pltpu.VMEM),
        ],
        out_specs=pl.BlockSpec(memory_space=pltpu.VMEM),
    )(a, b, x)


def _sorted_scatter_kernel(half, key_ref, slot_ref, side_ref, v_ref, o_ref):
    lanes = o_ref.shape[2]
    step = 64

    @pl.loop(0, o_ref.shape[0] // step)
    def _(i):
        at = pl.ds(pl.multiple_of(i * step, step), step)
        o_ref[at] = jnp.zeros((step,) + o_ref.shape[1:], o_ref.dtype)
    group = (lax.broadcasted_iota(jnp.int32, (1, lanes), 1) // half) % 2

    def body(t, carry):
        run, prev = carry
        base = t * BLOCK
        rows = [v_ref[slot_ref[base + r]] for r in range(BLOCK)]
        for r in range(BLOCK):
            i = base + r
            k = key_ref[i]
            mine = jnp.where(group == side_ref[i], rows[r], jnp.zeros_like(rows[r]))
            run = jnp.where(k == prev, run, jnp.zeros_like(run)) + mine
            o_ref[k] = run
            prev = k
        return run, prev

    lax.fori_loop(
        0,
        key_ref.shape[0] // BLOCK,
        body,
        (jnp.zeros((1, lanes), jnp.float32), jnp.int32(-1)),
    )


def sorted_scatter(half, key, slot, side, vals, rows):
    return pl.pallas_call(
        functools.partial(_sorted_scatter_kernel, half),
        out_shape=jax.ShapeDtypeStruct((rows,) + vals.shape[1:], vals.dtype),
        in_specs=[
            pl.BlockSpec(memory_space=pltpu.SMEM),
            pl.BlockSpec(memory_space=pltpu.SMEM),
            pl.BlockSpec(memory_space=pltpu.SMEM),
            pl.BlockSpec(memory_space=pltpu.VMEM),
        ],
        out_specs=pl.BlockSpec(memory_space=pltpu.VMEM),
    )(key, slot, side, vals)


def local(src_local, dst_local, edge_weight, send_counts, sketch):
    peers = lax.axis_size("dom")
    edges = src_local.shape[0]
    cap = edges // peers
    width = sketch.shape[0]

    def a2a(x):
        return lax.all_to_all(x, "dom", split_axis=0, concat_axis=0, tiled=True)

    live = (jnp.arange(cap)[None, :] < send_counts.reshape(peers, 1)).astype(jnp.float32)
    w_out = (edge_weight.reshape(peers, cap) * live).reshape(-1)
    root = jnp.sqrt(w_out)[:, None] * sketch.astype(jnp.float32).T
    lanes = 2 * width
    side_row = jnp.concatenate(
        [
            w_out.reshape(peers, 1, cap),
            dst_local.astype(jnp.float32).reshape(peers, 1, cap),
            jnp.zeros((peers, 1, lanes - 2 * cap), jnp.float32),
        ],
        axis=2,
    )
    payload = jnp.concatenate([root.reshape(peers, -1, lanes), side_row], axis=1)
    arrived = a2a(payload)
    arrived_root = arrived[:, :-1].reshape(edges, width)
    w_in = arrived[:, -1, :cap].reshape(-1)
    wanted = arrived[:, -1, cap:2 * cap].reshape(-1).astype(jnp.int32)

    keys = jnp.stack([src_local, wanted], axis=1).reshape(-1)
    key_s, entry_s = lax.sort(
        (keys, jnp.arange(2 * edges, dtype=jnp.int32)), num_keys=1
    )
    slot_s = entry_s // 2
    side_s = entry_s % 2

    def scatter(vals):
        return sorted_scatter(width, key_s, slot_s, side_s, vals, VERT_DEV).reshape(
            VERT_DEV, -1
        )

    ones = jnp.ones((1, width), jnp.float32)
    acc = scatter(
        jnp.concatenate(
            [root, -arrived_root, w_out[:, None] * ones, w_in[:, None] * ones], axis=1
        ).reshape(edges, 1, 2 * lanes)
    )
    rhs = acc[:, :width] + acc[:, width:lanes]
    degree = acc[:, lanes] + acc[:, lanes + width]
    diag = ((1.0 + degree_boost) * degree + ground_shift)[:, None]
    extra = (degree_boost * degree + ground_shift)[:, None]

    def ends(field):
        doubled = jnp.concatenate([field, field], axis=1).reshape(VERT_DEV, 1, 2 * width)
        return pair_gather(src_local, wanted, doubled)

    part = cap // CHUNKS

    def chunk(x, c):
        return x.reshape(peers, cap, -1)[:, c * part:(c + 1) * part].reshape(
            (peers * part,) + x.shape[1:]
        )

    parts = []
    for c in range(CHUNKS):
        src_c, wanted_c = chunk(src_local, c), chunk(wanted, c)
        keys_c = jnp.stack([src_c, wanted_c], axis=1).reshape(-1)
        key_c, entry_c = lax.sort(
            (keys_c, jnp.arange(2 * peers * part, dtype=jnp.int32)), num_keys=1
        )
        parts.append(
            (src_c, wanted_c, chunk(w_out, c), chunk(w_in, c), key_c, entry_c // 2, entry_c % 2)
        )

    def apply(field):
        doubled = jnp.concatenate([field, field], axis=1).reshape(VERT_DEV, 1, 2 * width)
        total = None
        for src_c, wanted_c, w_out_c, w_in_c, key_c, slot_c, side_c in parts:
            here = pair_gather(src_c, wanted_c, doubled)
            there = a2a(here).reshape(-1, 2 * width)
            here = here.reshape(-1, 2 * width)
            flow_out = w_out_c[:, None] * (here[:, :width] - there[:, width:])
            flow_in = w_in_c[:, None] * (there[:, :width] - here[:, width:])
            flows = jnp.concatenate([flow_out, -flow_in], axis=1).reshape(-1, 1, lanes)
            acc = sorted_scatter(width, key_c, slot_c, side_c, flows, VERT_DEV).reshape(
                VERT_DEV, lanes
            )
            total = acc if total is None else total + acc
        return (total[:, :width] + total[:, width:]) + extra * field

    sigma = 1.25
    delta = 0.8
    coeff = 1.0 / sigma
    resid = rhs
    direction = resid / diag
    solution = jnp.zeros((VERT_DEV, width), jnp.float32)
    for sweep in range(SWEEPS):
        solution = solution + direction
        if sweep < SWEEPS - 1:
            resid = resid - apply(direction)
            newer = 1.0 / (2.0 * sigma - coeff)
            direction = newer * coeff * direction + 2.0 * newer / delta * resid / diag
            coeff = newer
    here = ends(solution).reshape(edges, 2 * width)
    far = a2a(here[:, width:].reshape(edges // 2, 2 * width)).reshape(edges, width)
    diff = here[:, :width] - far
    partial_sum = jnp.sum(diff * diff, axis=1) * live.reshape(-1)
    resistance = lax.psum(partial_sum, "col") / SKETCH
    return (solution.T, resistance)


def solution(mesh):
    in_specs = (P("dom"), P("dom"), P("dom"), P("dom", None), P("col", "dom"))
    out_specs = (P("col", "dom"), P("dom"))
    return jax.shard_map(local, mesh=mesh, in_specs=in_specs, out_specs=out_specs, check_vma=False)
```

```python
import functools

import jax
import jax.numpy as jnp
from jax import lax
from jax.experimental import pallas as pl
from jax.experimental.pallas import tpu as pltpu
from jax.sharding import PartitionSpec as P

SKETCH = 128
VERT_DEV = 4096
SWEEPS = 3
BLOCK = 16


ground_shift = 1.0
degree_boost = 0.25


def _pair_gather_kernel(a_ref, b_ref, x_ref, o_ref):
    lanes = x_ref.shape[2]
    low = lax.broadcasted_iota(jnp.int32, (1, lanes), 1) < lanes // 2

    def body(t, carry):
        base = t * BLOCK
        rows = [(x_ref[a_ref[base + r]], x_ref[b_ref[base + r]]) for r in range(BLOCK)]
        for r in range(BLOCK):
            o_ref[base + r] = jnp.where(low, rows[r][0], rows[r][1])
        return carry

    lax.fori_loop(0, o_ref.shape[0] // BLOCK, body, 0)


def pair_gather(a, b, x):
    return pl.pallas_call(
        _pair_gather_kernel,
        out_shape=jax.ShapeDtypeStruct((a.shape[0],) + x.shape[1:], x.dtype),
        in_specs=[
            pl.BlockSpec(memory_space=pltpu.SMEM),
            pl.BlockSpec(memory_space=pltpu.SMEM),
            pl.BlockSpec(memory_space=pltpu.VMEM),
        ],
        out_specs=pl.BlockSpec(memory_space=pltpu.VMEM),
    )(a, b, x)


def _runs_kernel(key_ref, slot_ref, v_ref, o_ref):
    lanes = o_ref.shape[2]
    step = 64

    @pl.loop(0, o_ref.shape[0] // step)
    def _(i):
        at = pl.ds(pl.multiple_of(i * step, step), step)
        o_ref[at] = jnp.zeros((step,) + o_ref.shape[1:], o_ref.dtype)

    def body(t, carry):
        run, prev = carry
        base = t * BLOCK
        rows = [v_ref[slot_ref[base + r]] for r in range(BLOCK)]
        for r in range(BLOCK):
            k = key_ref[base + r]
            run = jnp.where(k == prev, run, jnp.zeros_like(run)) + rows[r]
            o_ref[k] = run
            prev = k
        return run, prev

    lax.fori_loop(
        0,
        key_ref.shape[0] // BLOCK,
        body,
        (jnp.zeros((1, lanes), jnp.float32), jnp.int32(-1)),
    )


def sorted_sum(key, slot, vals, rows):
    return pl.pallas_call(
        _runs_kernel,
        out_shape=jax.ShapeDtypeStruct((rows,) + vals.shape[1:], vals.dtype),
        in_specs=[
            pl.BlockSpec(memory_space=pltpu.SMEM),
            pl.BlockSpec(memory_space=pltpu.SMEM),
            pl.BlockSpec(memory_space=pltpu.VMEM),
        ],
        out_specs=pl.BlockSpec(memory_space=pltpu.VMEM),
    )(key, slot, vals).reshape(rows, -1)


def local(src_local, dst_local, edge_weight, send_counts, sketch):
    peers = lax.axis_size("dom")
    edges = src_local.shape[0]
    cap = edges // peers
    width = sketch.shape[0]

    def a2a(x):
        return lax.all_to_all(x, "dom", split_axis=0, concat_axis=0, tiled=True)

    live = (jnp.arange(cap)[None, :] < send_counts.reshape(peers, 1)).astype(jnp.float32)
    w_out = (edge_weight.reshape(peers, cap) * live).reshape(-1)
    root = jnp.sqrt(w_out)[:, None] * sketch.astype(jnp.float32).T
    lanes = 2 * width
    ones = jnp.ones((1, width), jnp.float32)
    slots = jnp.arange(edges, dtype=jnp.int32)

    key_0, slot_0 = lax.sort((src_local, slots), num_keys=1)
    own = sorted_sum(
        key_0,
        slot_0,
        jnp.concatenate([root, w_out[:, None] * ones], axis=1).reshape(edges, 1, lanes),
        VERT_DEV,
    )

    side_row = jnp.concatenate(
        [
            w_out.reshape(peers, 1, cap),
            dst_local.astype(jnp.float32).reshape(peers, 1, cap),
            jnp.zeros((peers, 1, lanes - 2 * cap), jnp.float32),
        ],
        axis=2,
    )
    payload = jnp.concatenate([root.reshape(peers, -1, lanes), side_row], axis=1)
    arrived = a2a(payload)
    arrived_root = arrived[:, :-1].reshape(edges, width)
    w_in = arrived[:, -1, :cap].reshape(-1)
    wanted = arrived[:, -1, cap:2 * cap].reshape(-1).astype(jnp.int32)

    key_1, slot_1 = lax.sort((wanted, slots), num_keys=1)
    far = sorted_sum(
        key_1,
        slot_1,
        jnp.concatenate([-arrived_root, w_in[:, None] * ones], axis=1).reshape(
            edges, 1, lanes
        ),
        VERT_DEV,
    )
    rhs = own[:, :width] + far[:, :width]
    degree = own[:, width] + far[:, width]
    diag = ((1.0 + degree_boost) * degree + ground_shift)[:, None]
    extra = (degree_boost * degree + ground_shift)[:, None]

    def ends(field):
        doubled = jnp.concatenate([field, field], axis=1).reshape(VERT_DEV, 1, 2 * width)
        return pair_gather(src_local, wanted, doubled)

    def apply(field):
        here = ends(field)
        there = a2a(here).reshape(edges, 2 * width)
        here = here.reshape(edges, 2 * width)
        flow_out = w_out[:, None] * (here[:, :width] - there[:, width:])
        flow_in = w_in[:, None] * (there[:, :width] - here[:, width:])
        flows = jnp.concatenate([flow_out, -flow_in], axis=1).reshape(edges, 1, lanes)
        at_first = sorted_sum(key_0, slot_0, flows, VERT_DEV)
        at_second = sorted_sum(key_1, slot_1, flows, VERT_DEV)
        return (at_first[:, :width] + at_second[:, width:]) + extra * field

    sigma = 1.25
    delta = 0.8
    coeff = 1.0 / sigma
    resid = rhs
    direction = resid / diag
    solution = jnp.zeros((VERT_DEV, width), jnp.float32)
    for sweep in range(SWEEPS):
        solution = solution + direction
        if sweep < SWEEPS - 1:
            resid = resid - apply(direction)
            newer = 1.0 / (2.0 * sigma - coeff)
            direction = newer * coeff * direction + 2.0 * newer / delta * resid / diag
            coeff = newer
    here = ends(solution).reshape(edges, 2 * width)
    far = a2a(here[:, width:].reshape(edges // 2, 2 * width)).reshape(edges, width)
    diff = here[:, :width] - far
    partial_sum = jnp.sum(diff * diff, axis=1) * live.reshape(-1)
    resistance = lax.psum(partial_sum, "col") / SKETCH
    return (solution.T, resistance)


def solution(mesh):
    in_specs = (P("dom"), P("dom"), P("dom"), P("dom", None), P("col", "dom"))
    out_specs = (P("col", "dom"), P("dom"))
    return jax.shard_map(local, mesh=mesh, in_specs=in_specs, out_specs=out_specs, check_vma=False)
```

```python
import functools

import jax
import jax.numpy as jnp
from jax import lax
from jax.experimental import pallas as pl
from jax.experimental.pallas import tpu as pltpu
from jax.sharding import PartitionSpec as P

SKETCH = 128
VERT_DEV = 4096
SWEEPS = 3
BLOCK = 16


ground_shift = 1.0
degree_boost = 0.25


def _pair_gather_kernel(a_ref, b_ref, x_ref, o_ref):
    lanes = x_ref.shape[2]
    low = lax.broadcasted_iota(jnp.int32, (1, lanes), 1) < lanes // 2

    def body(t, carry):
        base = t * BLOCK
        rows = [(x_ref[a_ref[base + r]], x_ref[b_ref[base + r]]) for r in range(BLOCK)]
        for r in range(BLOCK):
            o_ref[base + r] = jnp.where(low, rows[r][0], rows[r][1])
        return carry

    lax.fori_loop(0, o_ref.shape[0] // BLOCK, body, 0)


def pair_gather(a, b, x):
    return pl.pallas_call(
        _pair_gather_kernel,
        out_shape=jax.ShapeDtypeStruct((a.shape[0],) + x.shape[1:], x.dtype),
        in_specs=[
            pl.BlockSpec(memory_space=pltpu.SMEM),
            pl.BlockSpec(memory_space=pltpu.SMEM),
            pl.BlockSpec(memory_space=pltpu.VMEM),
        ],
        out_specs=pl.BlockSpec(memory_space=pltpu.VMEM),
    )(a, b, x)


def _runs_kernel(key_ref, slot_ref, v_ref, o_ref):
    lanes = o_ref.shape[2]
    step = 64

    @pl.loop(0, o_ref.shape[0] // step)
    def _(i):
        at = pl.ds(pl.multiple_of(i * step, step), step)
        o_ref[at] = jnp.zeros((step,) + o_ref.shape[1:], o_ref.dtype)

    def body(t, carry):
        run, prev = carry
        base = t * BLOCK
        rows = [v_ref[slot_ref[base + r]] for r in range(BLOCK)]
        for r in range(BLOCK):
            k = key_ref[base + r]
            run = jnp.where(k == prev, run, jnp.zeros_like(run)) + rows[r]
            o_ref[k] = run
            prev = k
        return run, prev

    lax.fori_loop(
        0,
        key_ref.shape[0] // BLOCK,
        body,
        (jnp.zeros((1, lanes), jnp.float32), jnp.int32(-1)),
    )


def sorted_sum(key, slot, vals, rows):
    return pl.pallas_call(
        _runs_kernel,
        out_shape=jax.ShapeDtypeStruct((rows,) + vals.shape[1:], vals.dtype),
        in_specs=[
            pl.BlockSpec(memory_space=pltpu.SMEM),
            pl.BlockSpec(memory_space=pltpu.SMEM),
            pl.BlockSpec(memory_space=pltpu.VMEM),
        ],
        out_specs=pl.BlockSpec(memory_space=pltpu.VMEM),
    )(key, slot, vals).reshape(rows, -1)


def local(src_local, dst_local, edge_weight, send_counts, sketch):
    peers = lax.axis_size("dom")
    edges = src_local.shape[0]
    cap = edges // peers
    width = sketch.shape[0]

    def a2a(x):
        return lax.all_to_all(x, "dom", split_axis=0, concat_axis=0, tiled=True)

    live = (jnp.arange(cap)[None, :] < send_counts.reshape(peers, 1)).astype(jnp.float32)
    w_out = (edge_weight.reshape(peers, cap) * live).reshape(-1)
    root = jnp.sqrt(w_out)[:, None] * sketch.astype(jnp.float32).T
    lanes = 2 * width
    ones = jnp.ones((1, width), jnp.float32)
    slots = jnp.arange(edges, dtype=jnp.int32)

    key_0, slot_0 = lax.sort((src_local, slots), num_keys=1)
    own = sorted_sum(
        key_0,
        slot_0,
        jnp.concatenate([root, w_out[:, None] * ones], axis=1).reshape(edges, 1, lanes),
        VERT_DEV,
    )

    side_row = jnp.concatenate(
        [
            w_out.reshape(peers, 1, cap),
            dst_local.astype(jnp.float32).reshape(peers, 1, cap),
            jnp.zeros((peers, 1, lanes - 2 * cap), jnp.float32),
        ],
        axis=2,
    )
    payload = jnp.concatenate([root.reshape(peers, -1, lanes), side_row], axis=1)
    arrived = a2a(payload)
    arrived_root = arrived[:, :-1].reshape(edges, width)
    w_in = arrived[:, -1, :cap].reshape(-1)
    wanted = arrived[:, -1, cap:2 * cap].reshape(-1).astype(jnp.int32)

    key_1, slot_1 = lax.sort((wanted, slots), num_keys=1)
    far = sorted_sum(
        key_1,
        slot_1,
        jnp.concatenate([-arrived_root, w_in[:, None] * ones], axis=1).reshape(
            edges, 1, lanes
        ),
        VERT_DEV,
    )
    rhs = own[:, :width] + far[:, :width]
    degree = own[:, width] + far[:, width]
    diag = ((1.0 + degree_boost) * degree + ground_shift)[:, None]
    extra = (degree_boost * degree + ground_shift)[:, None]

    def ends(field):
        doubled = jnp.concatenate([field, field], axis=1).reshape(VERT_DEV, 1, 2 * width)
        return pair_gather(src_local, wanted, doubled)

    def apply(field):
        here = ends(field)
        there = a2a(here).reshape(edges, 2 * width)
        here = here.reshape(edges, 2 * width)
        flow_out = w_out[:, None] * (here[:, :width] - there[:, width:])
        flow_in = w_in[:, None] * (there[:, :width] - here[:, width:])
        flows = jnp.concatenate([flow_out, -flow_in], axis=1).reshape(edges, 1, lanes)
        at_first = sorted_sum(key_0, slot_0, flows, VERT_DEV)
        at_second = sorted_sum(key_1, slot_1, flows, VERT_DEV)
        return (at_first[:, :width] + at_second[:, width:]) + extra * field

    sigma = 1.25
    delta = 0.8
    coeff = 1.0 / sigma
    resid = rhs
    direction = resid / diag
    solution = jnp.zeros((VERT_DEV, width), jnp.float32)
    for sweep in range(SWEEPS):
        solution = solution + direction
        if sweep < SWEEPS - 1:
            resid = resid - apply(direction)
            newer = 1.0 / (2.0 * sigma - coeff)
            direction = newer * coeff * direction + 2.0 * newer / delta * resid / diag
            coeff = newer
    doubled = jnp.concatenate([solution, solution], axis=1).reshape(VERT_DEV, 1, lanes)
    far = a2a(pair_gather(wanted[0::2], wanted[1::2], doubled)).reshape(edges, width)
    near = pair_gather(src_local[0::2], src_local[1::2], doubled).reshape(edges, width)
    diff = near - far
    partial_sum = jnp.sum(diff * diff, axis=1) * live.reshape(-1)
    resistance = lax.psum(partial_sum, "col") / SKETCH
    return (solution.T, resistance)


def solution(mesh):
    in_specs = (P("dom"), P("dom"), P("dom"), P("dom", None), P("col", "dom"))
    out_specs = (P("col", "dom"), P("dom"))
    return jax.shard_map(local, mesh=mesh, in_specs=in_specs, out_specs=out_specs, check_vma=False)
```

```python
import functools

import jax
import jax.numpy as jnp
from jax import lax
from jax.experimental import pallas as pl
from jax.experimental.pallas import tpu as pltpu
from jax.sharding import PartitionSpec as P

SKETCH = 128
VERT_DEV = 4096
SWEEPS = 3
BLOCK = 16


ground_shift = 1.0
degree_boost = 0.25


def _pair_gather_kernel(a_ref, b_ref, x_ref, o_ref):
    lanes = x_ref.shape[2]
    low = lax.broadcasted_iota(jnp.int32, (1, lanes), 1) < lanes // 2

    def body(t, carry):
        base = t * BLOCK
        rows = [(x_ref[a_ref[base + r]], x_ref[b_ref[base + r]]) for r in range(BLOCK)]
        for r in range(BLOCK):
            o_ref[base + r] = jnp.where(low, rows[r][0], rows[r][1])
        return carry

    lax.fori_loop(0, o_ref.shape[0] // BLOCK, body, 0)


def pair_gather(a, b, x):
    return pl.pallas_call(
        _pair_gather_kernel,
        out_shape=jax.ShapeDtypeStruct((a.shape[0],) + x.shape[1:], x.dtype),
        in_specs=[
            pl.BlockSpec(memory_space=pltpu.SMEM),
            pl.BlockSpec(memory_space=pltpu.SMEM),
            pl.BlockSpec(memory_space=pltpu.VMEM),
        ],
        out_specs=pl.BlockSpec(memory_space=pltpu.VMEM),
    )(a, b, x)


def _runs_kernel(side, key_ref, slot_ref, v_ref, o_ref):
    lanes = o_ref.shape[2]
    low = lax.broadcasted_iota(jnp.int32, (1, lanes), 1) < lanes // 2
    step = 64

    @pl.loop(0, o_ref.shape[0] // step)
    def _(i):
        at = pl.ds(pl.multiple_of(i * step, step), step)
        o_ref[at] = jnp.zeros((step,) + o_ref.shape[1:], o_ref.dtype)

    def take(row):
        if side is None:
            return row
        turned = pltpu.roll(row, lanes // 2, 1)
        return jnp.where(low, row, turned) if side == 0 else jnp.where(low, turned, row)

    def body(t, carry):
        run, prev = carry
        base = t * BLOCK
        rows = [take(v_ref[slot_ref[base + r]]) for r in range(BLOCK)]
        for r in range(BLOCK):
            k = key_ref[base + r]
            run = jnp.where(k == prev, run, jnp.zeros_like(run)) + rows[r]
            o_ref[k] = run
            prev = k
        return run, prev

    lax.fori_loop(
        0,
        key_ref.shape[0] // BLOCK,
        body,
        (jnp.zeros((1, lanes), jnp.float32), jnp.int32(-1)),
    )


def sorted_sum(key, slot, vals, rows, side=None):
    return pl.pallas_call(
        functools.partial(_runs_kernel, side),
        out_shape=jax.ShapeDtypeStruct((rows,) + vals.shape[1:], vals.dtype),
        in_specs=[
            pl.BlockSpec(memory_space=pltpu.SMEM),
            pl.BlockSpec(memory_space=pltpu.SMEM),
            pl.BlockSpec(memory_space=pltpu.VMEM),
        ],
        out_specs=pl.BlockSpec(memory_space=pltpu.VMEM),
    )(key, slot, vals).reshape(rows, -1)


def local(src_local, dst_local, edge_weight, send_counts, sketch):
    peers = lax.axis_size("dom")
    edges = src_local.shape[0]
    cap = edges // peers
    width = sketch.shape[0]

    def a2a(x):
        return lax.all_to_all(x, "dom", split_axis=0, concat_axis=0, tiled=True)

    live = (jnp.arange(cap)[None, :] < send_counts.reshape(peers, 1)).astype(jnp.float32)
    w_out = (edge_weight.reshape(peers, cap) * live).reshape(-1)
    root = jnp.sqrt(w_out)[:, None] * sketch.astype(jnp.float32).T
    lanes = 2 * width
    ones = jnp.ones((1, width), jnp.float32)
    slots = jnp.arange(edges, dtype=jnp.int32)

    key_0, slot_0 = lax.sort((src_local, slots), num_keys=1)
    own = sorted_sum(
        key_0,
        slot_0,
        jnp.concatenate([root, w_out[:, None] * ones], axis=1).reshape(edges, 1, lanes),
        VERT_DEV,
    )

    side_row = jnp.concatenate(
        [
            w_out.reshape(peers, 1, cap),
            dst_local.astype(jnp.float32).reshape(peers, 1, cap),
            jnp.zeros((peers, 1, lanes - 2 * cap), jnp.float32),
        ],
        axis=2,
    )
    payload = jnp.concatenate([root.reshape(peers, -1, lanes), side_row], axis=1)
    arrived = a2a(payload)
    arrived_root = arrived[:, :-1].reshape(edges, width)
    w_in = arrived[:, -1, :cap].reshape(-1)
    wanted = arrived[:, -1, cap:2 * cap].reshape(-1).astype(jnp.int32)

    key_1, slot_1 = lax.sort((wanted, slots), num_keys=1)
    far = sorted_sum(
        key_1,
        slot_1,
        jnp.concatenate([-arrived_root, w_in[:, None] * ones], axis=1).reshape(
            edges, 1, lanes
        ),
        VERT_DEV,
    )
    rhs = own[:, :width] + far[:, :width]
    degree = own[:, width] + far[:, width]
    diag = ((1.0 + degree_boost) * degree + ground_shift)[:, None]
    extra = (degree_boost * degree + ground_shift)[:, None]

    def apply(field):
        here = pair_gather(src_local, wanted, field.reshape(VERT_DEV, 1, lanes))
        there = a2a(here).reshape(edges, lanes)
        here = here.reshape(edges, lanes)
        flow_out = w_out[:, None] * (here[:, :width] - there[:, width:])
        flow_in = w_in[:, None] * (there[:, :width] - here[:, width:])
        flows = jnp.concatenate([flow_out, -flow_in], axis=1).reshape(edges, 1, lanes)
        at_first = sorted_sum(key_0, slot_0, flows, VERT_DEV, side=0)
        at_second = sorted_sum(key_1, slot_1, flows, VERT_DEV, side=1)
        return (at_first + at_second) + extra * field

    sigma = 1.25
    delta = 0.8
    coeff = 1.0 / sigma
    resid = jnp.concatenate([rhs, rhs], axis=1)
    direction = resid / diag
    solution = jnp.zeros((VERT_DEV, lanes), jnp.float32)
    for sweep in range(SWEEPS):
        solution = solution + direction
        if sweep < SWEEPS - 1:
            resid = resid - apply(direction)
            newer = 1.0 / (2.0 * sigma - coeff)
            direction = newer * coeff * direction + 2.0 * newer / delta * resid / diag
            coeff = newer
    doubled = solution.reshape(VERT_DEV, 1, lanes)
    far = a2a(pair_gather(wanted[0::2], wanted[1::2], doubled)).reshape(edges, width)
    near = pair_gather(src_local[0::2], src_local[1::2], doubled).reshape(edges, width)
    diff = near - far
    partial_sum = jnp.sum(diff * diff, axis=1) * live.reshape(-1)
    resistance = lax.psum(partial_sum, "col") / SKETCH
    return (solution[:, :width].T, resistance)


def solution(mesh):
    in_specs = (P("dom"), P("dom"), P("dom"), P("dom", None), P("col", "dom"))
    out_specs = (P("col", "dom"), P("dom"))
    return jax.shard_map(local, mesh=mesh, in_specs=in_specs, out_specs=out_specs, check_vma=False)
```

```python
import functools

import jax
import jax.numpy as jnp
from jax import lax
from jax.experimental import pallas as pl
from jax.experimental.pallas import tpu as pltpu
from jax.sharding import PartitionSpec as P

SKETCH = 128
VERT_DEV = 4096
SWEEPS = 3
BLOCK = 16


ground_shift = 1.0
degree_boost = 0.25


def _pair_gather_kernel(a_ref, b_ref, x_ref, o_ref):
    lanes = x_ref.shape[2]
    low = lax.broadcasted_iota(jnp.int32, (1, lanes), 1) < lanes // 2

    def body(t, carry):
        base = t * BLOCK
        rows = [(x_ref[a_ref[base + r]], x_ref[b_ref[base + r]]) for r in range(BLOCK)]
        for r in range(BLOCK):
            o_ref[base + r] = jnp.where(low, rows[r][0], rows[r][1])
        return carry

    lax.fori_loop(0, o_ref.shape[0] // BLOCK, body, 0)


def pair_gather(a, b, x):
    return pl.pallas_call(
        _pair_gather_kernel,
        out_shape=jax.ShapeDtypeStruct((a.shape[0],) + x.shape[1:], x.dtype),
        in_specs=[
            pl.BlockSpec(memory_space=pltpu.SMEM),
            pl.BlockSpec(memory_space=pltpu.SMEM),
            pl.BlockSpec(memory_space=pltpu.VMEM),
        ],
        out_specs=pl.BlockSpec(memory_space=pltpu.VMEM),
    )(a, b, x)


def _runs_kernel(key_ref, slot_ref, v_ref, o_ref):
    lanes = o_ref.shape[2]
    step = 64

    @pl.loop(0, o_ref.shape[0] // step)
    def _(i):
        at = pl.ds(pl.multiple_of(i * step, step), step)
        o_ref[at] = jnp.zeros((step,) + o_ref.shape[1:], o_ref.dtype)

    def body(t, carry):
        run, prev = carry
        base = t * BLOCK
        rows = [v_ref[slot_ref[base + r]] for r in range(BLOCK)]
        for r in range(BLOCK):
            k = key_ref[base + r]
            run = jnp.where(k == prev, run, jnp.zeros_like(run)) + rows[r]
            o_ref[k] = run
            prev = k
        return run, prev

    lax.fori_loop(
        0,
        key_ref.shape[0] // BLOCK,
        body,
        (jnp.zeros((1, lanes), jnp.float32), jnp.int32(-1)),
    )


def sorted_sum(key, slot, vals, rows):
    return pl.pallas_call(
        _runs_kernel,
        out_shape=jax.ShapeDtypeStruct((rows,) + vals.shape[1:], vals.dtype),
        in_specs=[
            pl.BlockSpec(memory_space=pltpu.SMEM),
            pl.BlockSpec(memory_space=pltpu.SMEM),
            pl.BlockSpec(memory_space=pltpu.VMEM),
        ],
        out_specs=pl.BlockSpec(memory_space=pltpu.VMEM),
    )(key, slot, vals).reshape(rows, -1)


def local(src_local, dst_local, edge_weight, send_counts, sketch):
    peers = lax.axis_size("dom")
    edges = src_local.shape[0]
    cap = edges // peers
    width = sketch.shape[0]

    def a2a(x):
        return lax.all_to_all(x, "dom", split_axis=0, concat_axis=0, tiled=True)

    live = (jnp.arange(cap)[None, :] < send_counts.reshape(peers, 1)).astype(jnp.float32)
    w_out = (edge_weight.reshape(peers, cap) * live).reshape(-1)
    root = jnp.sqrt(w_out)[:, None] * sketch.astype(jnp.float32).T
    lanes = 2 * width
    ones = jnp.ones((1, width), jnp.float32)
    slots = jnp.arange(edges, dtype=jnp.int32)

    key_0, slot_0 = lax.sort((src_local, slots), num_keys=1)
    own = sorted_sum(
        key_0,
        slot_0,
        jnp.concatenate([root, w_out[:, None] * ones], axis=1).reshape(edges, 1, lanes),
        VERT_DEV,
    )

    side_row = jnp.concatenate(
        [
            w_out.reshape(peers, 1, cap),
            dst_local.astype(jnp.float32).reshape(peers, 1, cap),
            jnp.zeros((peers, 1, lanes - 2 * cap), jnp.float32),
        ],
        axis=2,
    )
    payload = jnp.concatenate([root.reshape(peers, -1, lanes), side_row], axis=1)
    arrived = a2a(payload)
    arrived_root = arrived[:, :-1].reshape(edges, width)
    w_in = arrived[:, -1, :cap].reshape(-1)
    wanted = arrived[:, -1, cap:2 * cap].reshape(-1).astype(jnp.int32)

    key_1, slot_1 = lax.sort((wanted, slots), num_keys=1)
    far = sorted_sum(
        key_1,
        slot_1,
        jnp.concatenate([-arrived_root, w_in[:, None] * ones], axis=1).reshape(
            edges, 1, lanes
        ),
        VERT_DEV,
    )
    rhs = own[:, :width] + far[:, :width]
    degree = own[:, width:] + far[:, width:]
    diag = (1.0 + degree_boost) * degree + ground_shift
    extra = degree_boost * degree + ground_shift

    def ends(field):
        doubled = jnp.concatenate([field, field], axis=1).reshape(VERT_DEV, 1, 2 * width)
        return pair_gather(src_local, wanted, doubled)

    def apply(field):
        here = ends(field)
        there = a2a(here).reshape(edges, 2 * width)
        here = here.reshape(edges, 2 * width)
        flow_out = w_out[:, None] * (here[:, :width] - there[:, width:])
        flow_in = w_in[:, None] * (there[:, :width] - here[:, width:])
        flows = jnp.concatenate([flow_out, -flow_in], axis=1).reshape(edges, 1, lanes)
        at_first = sorted_sum(key_0, slot_0, flows, VERT_DEV)
        at_second = sorted_sum(key_1, slot_1, flows, VERT_DEV)
        return (at_first[:, :width] + at_second[:, width:]) + extra * field

    sigma = 1.25
    delta = 0.8
    coeff = 1.0 / sigma
    resid = rhs
    direction = resid / diag
    solution = jnp.zeros((VERT_DEV, width), jnp.float32)
    for sweep in range(SWEEPS):
        solution = solution + direction
        if sweep < SWEEPS - 1:
            resid = resid - apply(direction)
            newer = 1.0 / (2.0 * sigma - coeff)
            direction = newer * coeff * direction + 2.0 * newer / delta * resid / diag
            coeff = newer
    doubled = jnp.concatenate([solution, solution], axis=1).reshape(VERT_DEV, 1, lanes)
    far = a2a(pair_gather(wanted[0::2], wanted[1::2], doubled)).reshape(edges, width)
    near = pair_gather(src_local[0::2], src_local[1::2], doubled).reshape(edges, width)
    diff = near - far
    partial_sum = jnp.sum(diff * diff, axis=1) * live.reshape(-1)
    resistance = lax.psum(partial_sum, "col") / SKETCH
    return (solution.T, resistance)


def solution(mesh):
    in_specs = (P("dom"), P("dom"), P("dom"), P("dom", None), P("col", "dom"))
    out_specs = (P("col", "dom"), P("dom"))
    return jax.shard_map(local, mesh=mesh, in_specs=in_specs, out_specs=out_specs, check_vma=False)
```

```python
import functools

import jax
import jax.numpy as jnp
from jax import lax
from jax.experimental import pallas as pl
from jax.experimental.pallas import tpu as pltpu
from jax.sharding import PartitionSpec as P

SKETCH = 128
VERT_DEV = 4096
SWEEPS = 3
BLOCK = 16


ground_shift = 1.0
degree_boost = 0.25


def _pair_gather_kernel(a_ref, b_ref, x_ref, o_ref):
    lanes = x_ref.shape[2]
    low = lax.broadcasted_iota(jnp.int32, (1, lanes), 1) < lanes // 2

    def body(t, carry):
        base = t * BLOCK
        rows = [(x_ref[a_ref[base + r]], x_ref[b_ref[base + r]]) for r in range(BLOCK)]
        for r in range(BLOCK):
            o_ref[base + r] = jnp.where(low, rows[r][0], rows[r][1])
        return carry

    lax.fori_loop(0, o_ref.shape[0] // BLOCK, body, 0)


def pair_gather(a, b, x):
    return pl.pallas_call(
        _pair_gather_kernel,
        out_shape=jax.ShapeDtypeStruct((a.shape[0],) + x.shape[1:], x.dtype),
        in_specs=[
            pl.BlockSpec(memory_space=pltpu.SMEM),
            pl.BlockSpec(memory_space=pltpu.SMEM),
            pl.BlockSpec(memory_space=pltpu.VMEM),
        ],
        out_specs=pl.BlockSpec(memory_space=pltpu.VMEM),
    )(a, b, x)


def _runs_kernel(key_ref, slot_ref, v_ref, o_ref):
    lanes = o_ref.shape[2]
    step = 64

    @pl.loop(0, o_ref.shape[0] // step)
    def _(i):
        at = pl.ds(pl.multiple_of(i * step, step), step)
        o_ref[at] = jnp.zeros((step,) + o_ref.shape[1:], o_ref.dtype)

    def body(t, carry):
        run, prev = carry
        base = t * BLOCK
        rows = [v_ref[slot_ref[base + r]] for r in range(BLOCK)]
        for r in range(BLOCK):
            k = key_ref[base + r]
            run = jnp.where(k == prev, run, jnp.zeros_like(run)) + rows[r]
            o_ref[k] = run
            prev = k
        return run, prev

    lax.fori_loop(
        0,
        key_ref.shape[0] // BLOCK,
        body,
        (jnp.zeros((1, lanes), jnp.float32), jnp.int32(-1)),
    )


def sorted_sum(key, slot, vals, rows):
    return pl.pallas_call(
        _runs_kernel,
        out_shape=jax.ShapeDtypeStruct((rows,) + vals.shape[1:], vals.dtype),
        in_specs=[
            pl.BlockSpec(memory_space=pltpu.SMEM),
            pl.BlockSpec(memory_space=pltpu.SMEM),
            pl.BlockSpec(memory_space=pltpu.VMEM),
        ],
        out_specs=pl.BlockSpec(memory_space=pltpu.VMEM),
    )(key, slot, vals).reshape(rows, -1)


def local(src_local, dst_local, edge_weight, send_counts, sketch):
    peers = lax.axis_size("dom")
    edges = src_local.shape[0]
    cap = edges // peers
    width = sketch.shape[0]

    def a2a(x):
        return lax.all_to_all(x, "dom", split_axis=0, concat_axis=0, tiled=True)

    live = (jnp.arange(cap)[None, :] < send_counts.reshape(peers, 1)).astype(jnp.float32)
    w_out = (edge_weight.reshape(peers, cap) * live).reshape(-1)
    root = jnp.sqrt(w_out)[:, None] * sketch.astype(jnp.float32).T
    lanes = 2 * width
    ones = jnp.ones((1, width), jnp.float32)
    slots = jnp.arange(edges, dtype=jnp.int32)

    key_0, slot_0 = lax.sort((src_local, slots), num_keys=1)
    own = sorted_sum(
        key_0,
        slot_0,
        jnp.concatenate([root, w_out[:, None] * ones], axis=1).reshape(edges, 1, lanes),
        VERT_DEV,
    )

    side_row = jnp.concatenate(
        [
            w_out.reshape(peers, 1, cap),
            dst_local.astype(jnp.float32).reshape(peers, 1, cap),
            jnp.zeros((peers, 1, lanes - 2 * cap), jnp.float32),
        ],
        axis=2,
    )
    payload = jnp.concatenate([root.reshape(peers, -1, lanes), side_row], axis=1)
    arrived = a2a(payload)
    arrived_root = arrived[:, :-1].reshape(edges, width)
    w_in = arrived[:, -1, :cap].reshape(-1)
    wanted = arrived[:, -1, cap:2 * cap].reshape(-1).astype(jnp.int32)

    key_1, slot_1 = lax.sort((wanted, slots), num_keys=1)
    far = sorted_sum(
        key_1,
        slot_1,
        jnp.concatenate([-arrived_root, w_in[:, None] * ones], axis=1).reshape(
            edges, 1, lanes
        ),
        VERT_DEV,
    )
    rhs = own[:, :width] + far[:, :width]
    degree = own[:, width] + far[:, width]
    diag = ((1.0 + degree_boost) * degree + ground_shift)[:, None]
    extra = (degree_boost * degree + ground_shift)[:, None]

    weights = jnp.concatenate([w_out[:, None] * ones, w_in[:, None] * ones], axis=1)

    def ends(field):
        doubled = jnp.concatenate([field, field], axis=1).reshape(VERT_DEV, 1, 2 * width)
        return pair_gather(src_local, wanted, doubled)

    def apply(field):
        here = ends(field)
        there = a2a(here).reshape(edges, 2 * width)
        here = here.reshape(edges, 2 * width)
        swapped = jnp.concatenate([there[:, width:], there[:, :width]], axis=1)
        flows = (weights * (here - swapped)).reshape(edges, 1, lanes)
        at_first = sorted_sum(key_0, slot_0, flows, VERT_DEV)
        at_second = sorted_sum(key_1, slot_1, flows, VERT_DEV)
        return (at_first[:, :width] + at_second[:, width:]) + extra * field

    sigma = 1.25
    delta = 0.8
    coeff = 1.0 / sigma
    resid = rhs
    direction = resid / diag
    solution = jnp.zeros((VERT_DEV, width), jnp.float32)
    for sweep in range(SWEEPS):
        solution = solution + direction
        if sweep < SWEEPS - 1:
            resid = resid - apply(direction)
            newer = 1.0 / (2.0 * sigma - coeff)
            direction = newer * coeff * direction + 2.0 * newer / delta * resid / diag
            coeff = newer
    doubled = jnp.concatenate([solution, solution], axis=1).reshape(VERT_DEV, 1, lanes)
    far = a2a(pair_gather(wanted[0::2], wanted[1::2], doubled)).reshape(edges, width)
    near = pair_gather(src_local[0::2], src_local[1::2], doubled).reshape(edges, width)
    diff = near - far
    partial_sum = jnp.sum(diff * diff, axis=1) * live.reshape(-1)
    resistance = lax.psum(partial_sum, "col") / SKETCH
    return (solution.T, resistance)


def solution(mesh):
    in_specs = (P("dom"), P("dom"), P("dom"), P("dom", None), P("col", "dom"))
    out_specs = (P("col", "dom"), P("dom"))
    return jax.shard_map(local, mesh=mesh, in_specs=in_specs, out_specs=out_specs, check_vma=False)
```

```python
import functools

import jax
import jax.numpy as jnp
from jax import lax
from jax.experimental import pallas as pl
from jax.experimental.pallas import tpu as pltpu
from jax.sharding import PartitionSpec as P

SKETCH = 128
VERT_DEV = 4096
SWEEPS = 3
BLOCK = 16


ground_shift = 1.0
degree_boost = 0.25


def _pair_gather_kernel(a_ref, b_ref, x_ref, o_ref):
    lanes = x_ref.shape[2]
    low = lax.broadcasted_iota(jnp.int32, (1, lanes), 1) < lanes // 2

    def body(t, carry):
        base = t * BLOCK
        rows = [(x_ref[a_ref[base + r]], x_ref[b_ref[base + r]]) for r in range(BLOCK)]
        for r in range(BLOCK):
            o_ref[base + r] = jnp.where(low, rows[r][0], rows[r][1])
        return carry

    lax.fori_loop(0, o_ref.shape[0] // BLOCK, body, 0)


def pair_gather(a, b, x):
    return pl.pallas_call(
        _pair_gather_kernel,
        out_shape=jax.ShapeDtypeStruct((a.shape[0],) + x.shape[1:], x.dtype),
        in_specs=[
            pl.BlockSpec(memory_space=pltpu.SMEM),
            pl.BlockSpec(memory_space=pltpu.SMEM),
            pl.BlockSpec(memory_space=pltpu.VMEM),
        ],
        out_specs=pl.BlockSpec(memory_space=pltpu.VMEM),
    )(a, b, x)


def _runs_kernel(key_ref, slot_ref, v_ref, o_ref):
    lanes = o_ref.shape[2]
    step = 64

    @pl.loop(0, o_ref.shape[0] // step)
    def _(i):
        at = pl.ds(pl.multiple_of(i * step, step), step)
        o_ref[at] = jnp.zeros((step,) + o_ref.shape[1:], o_ref.dtype)

    def body(t, carry):
        run, prev = carry
        base = t * BLOCK
        rows = [v_ref[slot_ref[base + r]] for r in range(BLOCK)]
        for r in range(BLOCK):
            k = key_ref[base + r]
            run = jnp.where(k == prev, run, jnp.zeros_like(run)) + rows[r]
            o_ref[k] = run
            prev = k
        return run, prev

    lax.fori_loop(
        0,
        key_ref.shape[0] // BLOCK,
        body,
        (jnp.zeros((1, lanes), jnp.float32), jnp.int32(-1)),
    )


def sorted_sum(key, slot, vals, rows):
    return pl.pallas_call(
        _runs_kernel,
        out_shape=jax.ShapeDtypeStruct((rows,) + vals.shape[1:], vals.dtype),
        in_specs=[
            pl.BlockSpec(memory_space=pltpu.SMEM),
            pl.BlockSpec(memory_space=pltpu.SMEM),
            pl.BlockSpec(memory_space=pltpu.VMEM),
        ],
        out_specs=pl.BlockSpec(memory_space=pltpu.VMEM),
    )(key, slot, vals).reshape(rows, -1)


def local(src_local, dst_local, edge_weight, send_counts, sketch):
    peers = lax.axis_size("dom")
    edges = src_local.shape[0]
    cap = edges // peers
    width = sketch.shape[0]

    def a2a(x):
        return lax.all_to_all(x, "dom", split_axis=0, concat_axis=0, tiled=True)

    live = (jnp.arange(cap)[None, :] < send_counts.reshape(peers, 1)).astype(jnp.float32)
    w_out = (edge_weight.reshape(peers, cap) * live).reshape(-1)
    root = jnp.sqrt(w_out)[:, None] * sketch.astype(jnp.float32).T
    lanes = 2 * width
    ones = jnp.ones((1, width), jnp.float32)
    slots = jnp.arange(edges, dtype=jnp.int32)

    key_0, slot_0 = lax.sort((src_local, slots), num_keys=1)
    own = sorted_sum(
        key_0,
        slot_0,
        jnp.concatenate([root, w_out[:, None] * ones], axis=1).reshape(edges, 1, lanes),
        VERT_DEV,
    )

    side_row = jnp.concatenate(
        [
            w_out.reshape(peers, 1, cap),
            dst_local.astype(jnp.float32).reshape(peers, 1, cap),
            jnp.zeros((peers, 1, lanes - 2 * cap), jnp.float32),
        ],
        axis=2,
    )
    payload = jnp.concatenate([root.reshape(peers, -1, lanes), side_row], axis=1)
    arrived = a2a(payload)
    arrived_root = arrived[:, :-1].reshape(edges, width)
    w_in = arrived[:, -1, :cap].reshape(-1)
    wanted = arrived[:, -1, cap:2 * cap].reshape(-1).astype(jnp.int32)

    key_1, slot_1 = lax.sort((wanted, slots), num_keys=1)
    far = sorted_sum(
        key_1,
        slot_1,
        jnp.concatenate([-arrived_root, w_in[:, None] * ones], axis=1).reshape(
            edges, 1, lanes
        ),
        VERT_DEV,
    )
    rhs = own[:, :width] + far[:, :width]
    degree = own[:, width] + far[:, width]
    diag = ((1.0 + degree_boost) * degree + ground_shift)[:, None]
    extra = (degree_boost * degree + ground_shift)[:, None]

    def ends(field):
        doubled = jnp.concatenate([field, field], axis=1).reshape(VERT_DEV, 1, 2 * width)
        return pair_gather(src_local, wanted, doubled)

    def apply(field):
        here = ends(field)
        there = a2a(here).reshape(edges, 2 * width)
        here = here.reshape(edges, 2 * width)
        flow_out = w_out[:, None] * (here[:, :width] - there[:, width:])
        flow_in = w_in[:, None] * (there[:, :width] - here[:, width:])
        flows = jnp.concatenate([flow_out, -flow_in], axis=1).reshape(edges, 1, lanes)
        at_first = sorted_sum(key_0, slot_0, flows, VERT_DEV)
        at_second = sorted_sum(key_1, slot_1, flows, VERT_DEV)
        return (at_first[:, :width] + at_second[:, width:]) + extra * field

    sigma = 1.25
    delta = 0.8
    coeff = 1.0 / sigma
    resid = rhs
    direction = resid / diag
    solution = jnp.zeros((VERT_DEV, width), jnp.float32)
    for sweep in range(SWEEPS):
        solution = solution + direction
        if sweep < SWEEPS - 1:
            resid = resid - apply(direction)
            newer = 1.0 / (2.0 * sigma - coeff)
            direction = newer * coeff * direction + 2.0 * newer / delta * resid / diag
            coeff = newer
    doubled = jnp.concatenate([solution, solution], axis=1).reshape(VERT_DEV, 1, lanes)
    far = a2a(pair_gather(wanted[0::2], wanted[1::2], doubled)).reshape(edges, width)
    near = pair_gather(src_local[0::2], src_local[1::2], doubled).reshape(edges, width)
    diff = near - far
    partial_sum = jnp.sum(diff * diff, axis=1) * live.reshape(-1)
    other = lax.ppermute(partial_sum, "col", [(0, 1), (1, 0)])
    resistance = (partial_sum + other) / SKETCH
    return (solution.T, resistance)


def solution(mesh):
    in_specs = (P("dom"), P("dom"), P("dom"), P("dom", None), P("col", "dom"))
    out_specs = (P("col", "dom"), P("dom"))
    return jax.shard_map(local, mesh=mesh, in_specs=in_specs, out_specs=out_specs, check_vma=False)
```
